512 devices in a mesh: filt: 64 (over y, x, z_hi), slab: 8 (over z_lo, core).
Axes of the slice: x: 4, y: 4, z: 16 (z_hi: 4, z_lo: 4; z = z_hi * 4 + z_lo), core: 2. Of those that a mesh axis runs over, the one named last changes fastest.
Arguments:
- activations: bfloat16 [2048, 16, 512], P('filt', 'slab'), may hold values from -6 to 6
- grad_out: bfloat16 [2048, 16, 512], P('filt', 'slab'), may hold values from -6 to 6
- weights: bfloat16 [27, 256, 256], P(None, 'filt'), may hold values from -0.078125 to 0.078125
Outputs:
- out_map: bfloat16 [2048, 16, 512], P('filt', 'slab')
- grad_in: bfloat16 [2048, 16, 512], P('filt', 'slab')
- filter_grad: float32 [27, 256, 256], P(None, 'filt')
The draws below stay inside these ranges and needn't reach their ends.
All inputs are finite; a program needn't handle non-finite values.
Results may differ from the reference program's by a relative error of at most 0.001.
Values may be sent and summed in bfloat16 or wider, within the bound.
No kernel may reach another device: no remote copies, remote signals or barrier semaphores. Data moves between devices by JAX's collectives and lax.ppermute only.
A program may use at most 64 MiB of HBM per device.

```python
import math
import jax
import jax.numpy as jnp
from jax import lax

CH_IN = 256
CH_OUT = 256
GROUPS = 8
ROWS = 8
WIDTH = 64
ROW_BLOCKS = 8
HEIGHT = 64
DEPTH_ALL = 16
N_FILT = 64


def block_scale(own_key, dims, shards, low, top_value):
    def one(position, blocks):
        steps = jax.random.uniform(jax.random.fold_in(jax.random.fold_in(own_key, 6), position), (blocks,), jnp.float32, low / len(shards), top_value / len(shards))
        return jnp.repeat(jnp.exp(steps), dims[position] // blocks).reshape((-1,) + (1,) * (len(dims) - position - 1))

    loudness = one(*shards[0])
    for cut in shards[1:]:
        loudness = loudness * one(*cut)
    return loudness


def centred(rng, shape, spread, reach, shards=(), kind=jnp.bfloat16):
    drawn = jax.random.normal(rng, shape, jnp.float32) * spread
    if len(shards) > 0:
        drawn = block_scale(rng, shape, shards, -0.22, 0.18) * drawn
    return jnp.clip(drawn, min=-reach, max=reach).astype(kind)


def setup_inputs(seed: int = 0) -> dict:
    key_of = jax.random.split(jax.random.key(seed), 4)
    return {
        "activations": centred(key_of[0], (ROW_BLOCKS * CH_IN, DEPTH_ALL, ROWS * WIDTH), 1.0, 6.0, ((0, 64), (1, 8))),
        "grad_out": centred(key_of[1], (ROW_BLOCKS * CH_OUT, DEPTH_ALL, ROWS * WIDTH), 1.0, 6.0, ((0, 64), (1, 8))),
        "weights": centred(key_of[2], (27, CH_OUT, CH_IN), (27 * CH_IN) ** -0.5, 0.078125, ((1, 64),)),
    }


def to_volume(array, chans):
    shaped = array.reshape(ROW_BLOCKS, GROUPS, chans // GROUPS, DEPTH_ALL, ROWS, WIDTH)
    return jnp.transpose(shaped, (1, 2, 3, 0, 4, 5)).reshape(chans, DEPTH_ALL, HEIGHT, WIDTH)

def from_volume(volume, chans):
    shaped = volume.reshape(GROUPS, chans // GROUPS, DEPTH_ALL, ROW_BLOCKS, ROWS, WIDTH)
    return jnp.transpose(shaped, (3, 0, 1, 2, 4, 5)).reshape(ROW_BLOCKS * chans, DEPTH_ALL, ROWS * WIDTH)

def rows_natural(array):
    shaped = array.reshape(27, ROW_BLOCKS, GROUPS, CH_OUT // N_FILT, CH_IN)
    return jnp.transpose(shaped, (0, 2, 1, 3, 4)).reshape(27, CH_OUT, CH_IN)

def rows_stored(array):
    shaped = array.reshape(27, GROUPS, ROW_BLOCKS, CH_OUT // N_FILT, CH_IN)
    return jnp.transpose(shaped, (0, 2, 1, 3, 4)).reshape(27, CH_OUT, CH_IN)

def shifted(padded, plane_off, row_off, col_off):
    window = padded[:, plane_off:plane_off + DEPTH_ALL, row_off:row_off + HEIGHT, col_off:col_off + WIDTH]
    return window.reshape(window.shape[0], -1)

def reference(activations, grad_out, weights):
    weights = rows_natural(weights)
    volume_in = to_volume(activations, CH_IN)
    volume_grad = to_volume(grad_out, CH_OUT)
    padded_in = jnp.pad(volume_in, ((0, 0), (1, 1), (1, 1), (1, 1)))
    padded_grad = jnp.pad(volume_grad, ((0, 0), (1, 1), (1, 1), (1, 1)))
    flat_grad = volume_grad.reshape(CH_OUT, -1)
    output_sum = jnp.zeros((CH_OUT, DEPTH_ALL * HEIGHT * WIDTH), jnp.float32)
    input_sum = jnp.zeros((CH_IN, DEPTH_ALL * HEIGHT * WIDTH), jnp.float32)
    filter_list = []
    for plane_off in range(3):
        for row_off in range(3):
            for col_off in range(3):
                tap = 9 * plane_off + 3 * row_off + col_off
                tap_input = shifted(padded_in, plane_off, row_off, col_off)
                output_sum = output_sum + jnp.dot(weights[tap], tap_input, preferred_element_type=jnp.float32)
                filter_list.append(lax.dot_general(flat_grad, tap_input, (((1,), (1,)), ((), ())), preferred_element_type=jnp.float32))
                tap_grad = shifted(padded_grad, 2 - plane_off, 2 - row_off, 2 - col_off)
                input_sum = input_sum + lax.dot_general(weights[tap], tap_grad, (((0,), (0,)), ((), ())), preferred_element_type=jnp.float32)
    scale_factor = 1.0 / math.sqrt(DEPTH_ALL * HEIGHT * WIDTH)
    filter_grad = rows_stored(jnp.stack(filter_list, axis=0) * scale_factor)
    out_map = from_volume(output_sum.astype(jnp.bfloat16).reshape(CH_OUT, DEPTH_ALL, HEIGHT, WIDTH), CH_OUT)
    grad_in = from_volume(input_sum.astype(jnp.bfloat16).reshape(CH_IN, DEPTH_ALL, HEIGHT, WIDTH), CH_IN)
    return (out_map, grad_in, filter_grad)
```

```python
import math

import jax
import jax.numpy as jnp
from jax import lax
from jax.sharding import Mesh
from jax.sharding import PartitionSpec as P

CH_IN = 256
CH_OUT = 256
GROUPS = 8
ROWS = 8
WIDTH = 64


def from_offset(value, d_rb, d_slab, n_rb, n_slab):
    if d_slab == 0:
        pairs = [(r + d_rb, r) for r in range(n_rb) if 0 <= r + d_rb < n_rb]
        return lax.ppermute(value, "rb", pairs)
    if d_rb == 0:
        pairs = [(s + d_slab, s) for s in range(n_slab) if 0 <= s + d_slab < n_slab]
        return lax.ppermute(value, "slab", pairs)
    pairs = []
    for r in range(n_rb):
        for s in range(n_slab):
            if 0 <= r + d_rb < n_rb and 0 <= s + d_slab < n_slab:
                pairs.append(((r + d_rb) * n_slab + s + d_slab, r * n_slab + s))
    return lax.ppermute(value, ("rb", "slab"), pairs)


def haloed(block):
    n_rb = lax.axis_size("rb")
    n_slab = lax.axis_size("slab")

    def part(d_rb, d_slab):
        piece = block
        if d_slab < 0:
            piece = piece[:, -1:]
        elif d_slab > 0:
            piece = piece[:, :1]
        if d_rb < 0:
            piece = piece[:, :, -1:]
        elif d_rb > 0:
            piece = piece[:, :, :1]
        if d_rb == 0 and d_slab == 0:
            return piece
        return from_offset(piece, d_rb, d_slab, n_rb, n_slab)

    planes = []
    for d_slab in (-1, 0, 1):
        planes.append(jnp.concatenate([part(d_rb, d_slab) for d_rb in (-1, 0, 1)], axis=2))
    return jnp.concatenate(planes, axis=1)


def correlate(image, kernel, lhs_spec):
    return lax.conv_general_dilated(
        image,
        kernel,
        (1, 1, 1),
        ((0, 0), (0, 0), (1, 1)),
        dimension_numbers=(lhs_spec, "OIDHW", "NCDHW"),
        preferred_element_type=jnp.float32,
    )


def per_device(activations, grad_out, weights):
    chan_local = activations.shape[0]
    depth_dev = activations.shape[1]
    n_rb = lax.axis_size("rb")
    depth_all = depth_dev * lax.axis_size("slab")
    height_all = ROWS * n_rb

    both = jnp.concatenate([activations, grad_out], axis=0).reshape(2 * chan_local, depth_dev, ROWS, WIDTH)
    whole = lax.all_gather(haloed(both), "grp", axis=0, tiled=False)
    whole_in = whole[:, :chan_local].reshape((CH_IN,) + whole.shape[2:])
    whole_grad = whole[:, chan_local:].reshape((CH_OUT,) + whole.shape[2:])

    group_weights = lax.all_gather(weights, "rb", axis=1, tiled=True)
    column_weights = lax.all_to_all(group_weights, "grp", split_axis=2, concat_axis=1, tiled=True)

    out_kernel = jnp.transpose(group_weights, (1, 2, 0)).reshape(chan_local, CH_IN, 3, 3, 3)
    output_sum = correlate(whole_in[None], out_kernel, "NCDHW")
    grad_kernel = grad_out.reshape(chan_local, 1, depth_dev, ROWS, WIDTH)
    filter_terms = correlate(whole_in[:, None], grad_kernel, "NCDHW")
    filter_part = jnp.transpose(filter_terms.reshape(CH_IN, chan_local, 27), (2, 1, 0))
    in_kernel = jnp.transpose(column_weights[::-1], (2, 1, 0)).reshape(chan_local, CH_OUT, 3, 3, 3)
    input_sum = correlate(whole_grad[None], in_kernel, "NCDHW")

    scale_factor = 1.0 / math.sqrt(depth_all * height_all * WIDTH)
    rows_part = lax.psum_scatter(filter_part, "rb", scatter_dimension=1, tiled=True)
    filter_grad = lax.psum(rows_part, "slab") * scale_factor
    out_map = output_sum.astype(jnp.bfloat16).reshape(chan_local, depth_dev, ROWS * WIDTH)
    grad_in = input_sum.astype(jnp.bfloat16).reshape(chan_local, depth_dev, ROWS * WIDTH)
    return (out_map, grad_in, filter_grad)


def solution(mesh):
    n_filt, n_slab = mesh.devices.shape
    grid = Mesh(mesh.devices.reshape(n_filt // GROUPS, GROUPS, n_slab), ("rb", "grp", "slab"))
    act_spec = P(("rb", "grp"), "slab", None)
    w_spec = P(None, ("rb", "grp"), None)
    in_specs = (act_spec, act_spec, w_spec)
    out_specs = (act_spec, act_spec, w_spec)
    return jax.shard_map(
        per_device, mesh=grid, in_specs=in_specs, out_specs=out_specs, check_vma=False
    )
```

```python
import math

import jax
import jax.numpy as jnp
from jax import lax
from jax.sharding import Mesh
from jax.sharding import PartitionSpec as P

CH_IN = 256
CH_OUT = 256
GROUPS = 8
ROWS = 8
WIDTH = 64


def from_offset(value, d_rb, d_slab, n_rb, n_slab):
    if d_slab == 0:
        pairs = [(r + d_rb, r) for r in range(n_rb) if 0 <= r + d_rb < n_rb]
        return lax.ppermute(value, "rb", pairs)
    if d_rb == 0:
        pairs = [(s + d_slab, s) for s in range(n_slab) if 0 <= s + d_slab < n_slab]
        return lax.ppermute(value, "slab", pairs)
    pairs = []
    for r in range(n_rb):
        for s in range(n_slab):
            if 0 <= r + d_rb < n_rb and 0 <= s + d_slab < n_slab:
                pairs.append(((r + d_rb) * n_slab + s + d_slab, r * n_slab + s))
    return lax.ppermute(value, ("rb", "slab"), pairs)


def haloed(block):
    n_rb = lax.axis_size("rb")
    n_slab = lax.axis_size("slab")

    def part(d_rb, d_slab):
        piece = block
        if d_slab < 0:
            piece = piece[:, -1:]
        elif d_slab > 0:
            piece = piece[:, :1]
        if d_rb < 0:
            piece = piece[:, :, -1:]
        elif d_rb > 0:
            piece = piece[:, :, :1]
        if d_rb == 0 and d_slab == 0:
            return piece
        return from_offset(piece, d_rb, d_slab, n_rb, n_slab)

    planes = []
    for d_slab in (-1, 0, 1):
        planes.append(jnp.concatenate([part(d_rb, d_slab) for d_rb in (-1, 0, 1)], axis=2))
    return jnp.concatenate(planes, axis=1)


def correlate(image, kernel, lhs_spec):
    return lax.conv_general_dilated(
        image,
        kernel,
        (1, 1, 1),
        ((0, 0), (0, 0), (1, 1)),
        dimension_numbers=(lhs_spec, "OIDHW", "NCDHW"),
        preferred_element_type=jnp.float32,
    )


def cyclic_from(value, axis, step):
    count = lax.axis_size(axis)
    return lax.ppermute(value, axis, [((i + step) % count, i) for i in range(count)])


def in_order(received, axis):
    return jnp.roll(received, lax.axis_index(axis), axis=0)


def per_device(activations, grad_out, weights):
    chan_local = activations.shape[0]
    depth_dev = activations.shape[1]
    rows_dev = weights.shape[1]
    n_rb = lax.axis_size("rb")
    n_grp = lax.axis_size("grp")
    n_slab = lax.axis_size("slab")
    depth_all = depth_dev * n_slab
    height_all = ROWS * n_rb
    my_grp = lax.axis_index("grp")
    my_rb = lax.axis_index("rb")

    both = jnp.concatenate([activations, grad_out], axis=0).reshape(2 * chan_local, depth_dev, ROWS, WIDTH)
    ext = haloed(both)
    ext_size = ext.size

    rows_from = [weights] + [cyclic_from(weights, "rb", k) for k in range(1, n_rb)]
    group_weights = in_order(jnp.stack(rows_from), "rb")
    group_weights = jnp.transpose(group_weights, (1, 0, 2, 3)).reshape(27, n_rb * rows_dev, CH_IN)

    def column_slice(target):
        return lax.dynamic_slice_in_dim(group_weights, target * chan_local, chan_local, axis=2)

    col_shape = (27, n_rb * rows_dev, chan_local)
    own = jnp.concatenate([ext.reshape(-1), column_slice(my_grp).reshape(-1)])
    pieces = [own]
    for k in range(1, n_grp):
        sent = jnp.concatenate([ext.reshape(-1), column_slice((my_grp - k) % n_grp).reshape(-1)])
        pieces.append(cyclic_from(sent, "grp", k))
    pieces = in_order(jnp.stack(pieces), "grp")
    whole = pieces[:, :ext_size].reshape((n_grp,) + ext.shape)
    whole_in = whole[:, :chan_local].reshape((CH_IN,) + ext.shape[1:])
    whole_grad = whole[:, chan_local:].reshape((CH_OUT,) + ext.shape[1:])
    column_weights = pieces[:, ext_size:].reshape((n_grp,) + col_shape)
    column_weights = jnp.transpose(column_weights, (1, 0, 2, 3)).reshape(27, CH_OUT, chan_local)

    out_kernel = jnp.transpose(group_weights, (1, 2, 0)).reshape(chan_local, CH_IN, 3, 3, 3)
    output_sum = correlate(whole_in[None], out_kernel, "NCDHW")
    grad_kernel = grad_out.reshape(chan_local, 1, depth_dev, ROWS, WIDTH)
    filter_terms = correlate(whole_in[:, None], grad_kernel, "NCDHW")
    filter_part = jnp.transpose(filter_terms.reshape(CH_IN, chan_local, 27), (2, 1, 0))
    in_kernel = jnp.transpose(column_weights[::-1], (2, 1, 0)).reshape(chan_local, CH_OUT, 3, 3, 3)
    input_sum = correlate(whole_grad[None], in_kernel, "NCDHW")

    def row_chunk(target):
        return lax.dynamic_slice_in_dim(filter_part, target * rows_dev, rows_dev, axis=1)

    sums = [row_chunk(my_rb)]
    for k in range(1, n_rb):
        sums.append(cyclic_from(row_chunk((my_rb - k) % n_rb), "rb", k))
    rows_part = jnp.sum(jnp.stack(sums), axis=0)
    slabs = [rows_part] + [cyclic_from(rows_part, "slab", k) for k in range(1, n_slab)]
    scale_factor = 1.0 / math.sqrt(depth_all * height_all * WIDTH)
    filter_grad = jnp.sum(in_order(jnp.stack(slabs), "slab"), axis=0) * scale_factor
    out_map = output_sum.astype(jnp.bfloat16).reshape(chan_local, depth_dev, ROWS * WIDTH)
    grad_in = input_sum.astype(jnp.bfloat16).reshape(chan_local, depth_dev, ROWS * WIDTH)
    return (out_map, grad_in, filter_grad)


def solution(mesh):
    n_filt, n_slab = mesh.devices.shape
    grid = Mesh(mesh.devices.reshape(n_filt // GROUPS, GROUPS, n_slab), ("rb", "grp", "slab"))
    act_spec = P(("rb", "grp"), "slab", None)
    w_spec = P(None, ("rb", "grp"), None)
    in_specs = (act_spec, act_spec, w_spec)
    out_specs = (act_spec, act_spec, w_spec)
    return jax.shard_map(
        per_device, mesh=grid, in_specs=in_specs, out_specs=out_specs, check_vma=False
    )
```

```python
import math

import jax
import jax.numpy as jnp
from jax import lax
from jax.sharding import Mesh
from jax.sharding import PartitionSpec as P

CH_IN = 256
CH_OUT = 256
GROUPS = 8
ROWS = 8
WIDTH = 64


def from_offset(value, d_rb, d_slab, n_rb, n_slab):
    if d_slab == 0:
        pairs = [(r + d_rb, r) for r in range(n_rb) if 0 <= r + d_rb < n_rb]
        return lax.ppermute(value, "rb", pairs)
    if d_rb == 0:
        pairs = [(s + d_slab, s) for s in range(n_slab) if 0 <= s + d_slab < n_slab]
        return lax.ppermute(value, "slab", pairs)
    pairs = []
    for r in range(n_rb):
        for s in range(n_slab):
            if 0 <= r + d_rb < n_rb and 0 <= s + d_slab < n_slab:
                pairs.append(((r + d_rb) * n_slab + s + d_slab, r * n_slab + s))
    return lax.ppermute(value, ("rb", "slab"), pairs)


def haloed(block):
    n_rb = lax.axis_size("rb")
    n_slab = lax.axis_size("slab")

    def part(d_rb, d_slab):
        piece = block
        if d_slab < 0:
            piece = piece[:, -1:]
        elif d_slab > 0:
            piece = piece[:, :1]
        if d_rb < 0:
            piece = piece[:, :, -1:]
        elif d_rb > 0:
            piece = piece[:, :, :1]
        if d_rb == 0 and d_slab == 0:
            return piece
        return from_offset(piece, d_rb, d_slab, n_rb, n_slab)

    planes = []
    for d_slab in (-1, 0, 1):
        planes.append(jnp.concatenate([part(d_rb, d_slab) for d_rb in (-1, 0, 1)], axis=2))
    return jnp.concatenate(planes, axis=1)


def correlate(image, kernel, lhs_spec):
    return lax.conv_general_dilated(
        image,
        kernel,
        (1, 1, 1),
        ((0, 0), (0, 0), (1, 1)),
        dimension_numbers=(lhs_spec, "OIDHW", "NCDHW"),
        preferred_element_type=jnp.float32,
    )


def cyclic_from(value, axis, step):
    count = lax.axis_size(axis)
    return lax.ppermute(value, axis, [((i + step) % count, i) for i in range(count)])


def in_order(received, axis):
    return jnp.roll(received, lax.axis_index(axis), axis=0)


def gathered(value, axis):
    received = [value] + [cyclic_from(value, axis, k) for k in range(1, lax.axis_size(axis))]
    return in_order(jnp.stack(received), axis)


def per_device(activations, grad_out, weights):
    chan_local = activations.shape[0]
    depth_dev = activations.shape[1]
    rows_dev = weights.shape[1]
    n_rb = lax.axis_size("rb")
    n_grp = lax.axis_size("grp")
    n_slab = lax.axis_size("slab")
    depth_all = depth_dev * n_slab
    height_all = ROWS * n_rb
    my_grp = lax.axis_index("grp")
    my_rb = lax.axis_index("rb")

    both = jnp.concatenate([activations, grad_out], axis=0)
    whole = gathered(both, "grp").reshape(n_grp * 2 * chan_local, depth_dev, ROWS, WIDTH)
    ext = haloed(whole).reshape((n_grp, 2, chan_local, depth_dev + 2, ROWS + 2, WIDTH))
    whole_in = ext[:, 0].reshape((CH_IN,) + ext.shape[3:])
    whole_grad = ext[:, 1].reshape((CH_OUT,) + ext.shape[3:])

    group_weights = gathered(weights, "rb")
    group_weights = jnp.transpose(group_weights, (1, 0, 2, 3)).reshape(27, n_rb * rows_dev, CH_IN)

    by_cols = jnp.transpose(weights.reshape(27, rows_dev, n_grp, chan_local), (2, 0, 1, 3))
    col_parts = [by_cols[my_grp]]
    for k in range(1, n_grp):
        col_parts.append(cyclic_from(by_cols[(my_grp - k) % n_grp], "grp", k))
    col_parts = in_order(jnp.stack(col_parts), "grp")
    column_weights = gathered(col_parts, "rb")
    column_weights = jnp.transpose(column_weights, (2, 1, 0, 3, 4)).reshape(27, CH_OUT, chan_local)

    out_kernel = jnp.transpose(group_weights, (1, 2, 0)).reshape(chan_local, CH_IN, 3, 3, 3)
    output_sum = correlate(whole_in[None], out_kernel, "NCDHW")
    grad_kernel = grad_out.reshape(chan_local, 1, depth_dev, ROWS, WIDTH)
    filter_terms = correlate(whole_in[:, None], grad_kernel, "NCDHW")
    filter_part = jnp.transpose(filter_terms.reshape(CH_IN, chan_local, 27), (2, 1, 0))
    in_kernel = jnp.transpose(column_weights[::-1], (2, 1, 0)).reshape(chan_local, CH_OUT, 3, 3, 3)
    input_sum = correlate(whole_grad[None], in_kernel, "NCDHW")

    def row_chunk(target):
        return lax.dynamic_slice_in_dim(filter_part, target * rows_dev, rows_dev, axis=1)

    sums = [row_chunk(my_rb)]
    for k in range(1, n_rb):
        sums.append(cyclic_from(row_chunk((my_rb - k) % n_rb), "rb", k))
    rows_part = jnp.sum(jnp.stack(sums), axis=0)
    scale_factor = 1.0 / math.sqrt(depth_all * height_all * WIDTH)
    filter_grad = jnp.sum(gathered(rows_part, "slab"), axis=0) * scale_factor
    out_map = output_sum.astype(jnp.bfloat16).reshape(chan_local, depth_dev, ROWS * WIDTH)
    grad_in = input_sum.astype(jnp.bfloat16).reshape(chan_local, depth_dev, ROWS * WIDTH)
    return (out_map, grad_in, filter_grad)


def solution(mesh):
    n_filt, n_slab = mesh.devices.shape
    grid = Mesh(mesh.devices.reshape(n_filt // GROUPS, GROUPS, n_slab), ("rb", "grp", "slab"))
    act_spec = P(("rb", "grp"), "slab", None)
    w_spec = P(None, ("rb", "grp"), None)
    in_specs = (act_spec, act_spec, w_spec)
    out_specs = (act_spec, act_spec, w_spec)
    return jax.shard_map(
        per_device, mesh=grid, in_specs=in_specs, out_specs=out_specs, check_vma=False
    )
```

```python
import math

import jax
import jax.numpy as jnp
from jax import lax
from jax.sharding import Mesh
from jax.sharding import PartitionSpec as P

CH_IN = 256
CH_OUT = 256
GROUPS = 8
ROWS = 8
WIDTH = 64


def linear_from(value, axis, step):
    count = lax.axis_size(axis)
    return lax.ppermute(value, axis, [(i + step, i) for i in range(count) if 0 <= i + step < count])


def haloed(block):
    deep = jnp.concatenate(
        [linear_from(block[:, -1:], "slab", -1), block, linear_from(block[:, :1], "slab", 1)], axis=1
    )
    return jnp.concatenate(
        [linear_from(deep[:, :, -1:], "rb", -1), deep, linear_from(deep[:, :, :1], "rb", 1)], axis=2
    )


def correlate(image, kernel, lhs_spec):
    return lax.conv_general_dilated(
        image,
        kernel,
        (1, 1, 1),
        ((0, 0), (0, 0), (1, 1)),
        dimension_numbers=(lhs_spec, "OIDHW", "NCDHW"),
        preferred_element_type=jnp.float32,
    )


def partner(value, axis, bit):
    count = lax.axis_size(axis)
    return lax.ppermute(value, axis, [(i, i ^ (1 << bit)) for i in range(count)])


def bit_of(axis, bit):
    return (lax.axis_index(axis) >> bit) % 2 == 1


def xor_gather(value, axis, bits):
    for bit in bits:
        other = partner(value, axis, bit)
        upper = bit_of(axis, bit)
        value = jnp.stack([jnp.where(upper, other, value), jnp.where(upper, value, other)])
    order = sorted(range(len(bits)), key=lambda j: -bits[len(bits) - 1 - j])
    value = jnp.transpose(value, order + list(range(len(bits), value.ndim)))
    return value.reshape((-1,) + value.shape[len(bits):])


def xor_scatter_sum(value, axis, bits):
    nbits = len(bits)
    value = value.reshape((2,) * nbits + value.shape[1:])
    for bit in bits:
        dim = nbits - 1 - bit
        upper = bit_of(axis, bit)
        low = lax.index_in_dim(value, 0, axis=dim, keepdims=True)
        high = lax.index_in_dim(value, 1, axis=dim, keepdims=True)
        keep = jnp.where(upper, high, low)
        sent = jnp.where(upper, low, high)
        value = keep + partner(sent, axis, bit)
    return value.reshape(value.shape[nbits:])


def xor_all_sum(value, axis, bits):
    for bit in bits:
        value = value + partner(value, axis, bit)
    return value


def per_device(activations, grad_out, weights):
    chan_local = activations.shape[0]
    depth_dev = activations.shape[1]
    rows_dev = weights.shape[1]
    n_rb = lax.axis_size("rb")
    n_slab = lax.axis_size("slab")
    depth_all = depth_dev * n_slab
    height_all = ROWS * n_rb

    all_in = xor_gather(activations, "grp", (1, 0, 2)).reshape(CH_IN, depth_dev, ROWS * WIDTH)
    both = jnp.concatenate([all_in, grad_out], axis=0).reshape(CH_IN + chan_local, depth_dev, ROWS, WIDTH)
    ext = haloed(both)
    whole_in = ext[:CH_IN]
    own_grad = ext[CH_IN:]

    group_weights = xor_gather(weights, "rb", (0, 2, 1))
    group_weights = jnp.transpose(group_weights, (1, 0, 2, 3)).reshape(27, n_rb * rows_dev, CH_IN)

    out_kernel = jnp.transpose(group_weights, (1, 2, 0)).reshape(chan_local, CH_IN, 3, 3, 3)
    output_sum = correlate(whole_in[None], out_kernel, "NCDHW")
    grad_kernel = grad_out.reshape(chan_local, 1, depth_dev, ROWS, WIDTH)
    filter_terms = correlate(whole_in[:, None], grad_kernel, "NCDHW")
    filter_part = jnp.transpose(filter_terms.reshape(CH_IN, chan_local, 27), (2, 1, 0))
    in_kernel = jnp.transpose(group_weights[::-1], (2, 1, 0)).reshape(CH_IN, chan_local, 3, 3, 3)
    input_terms = correlate(own_grad[None], in_kernel, "NCDHW").reshape(GROUPS, chan_local, depth_dev, ROWS * WIDTH)
    input_sum = xor_scatter_sum(input_terms, "grp", (2, 0, 1))

    rows_terms = jnp.moveaxis(filter_part.reshape(27, n_rb, rows_dev, CH_IN), 1, 0)
    rows_part = xor_scatter_sum(rows_terms, "rb", (1, 0, 2))
    scale_factor = 1.0 / math.sqrt(depth_all * height_all * WIDTH)
    filter_grad = xor_all_sum(rows_part, "slab", (0, 1, 2)) * scale_factor
    out_map = output_sum.astype(jnp.bfloat16).reshape(chan_local, depth_dev, ROWS * WIDTH)
    grad_in = input_sum.astype(jnp.bfloat16)
    return (out_map, grad_in, filter_grad)


def solution(mesh):
    n_filt, n_slab = mesh.devices.shape
    grid = Mesh(mesh.devices.reshape(n_filt // GROUPS, GROUPS, n_slab), ("rb", "grp", "slab"))
    act_spec = P(("rb", "grp"), "slab", None)
    w_spec = P(None, ("rb", "grp"), None)
    in_specs = (act_spec, act_spec, w_spec)
    out_specs = (act_spec, act_spec, w_spec)
    return jax.shard_map(
        per_device, mesh=grid, in_specs=in_specs, out_specs=out_specs, check_vma=False
    )
```

```python
import math

import jax
import jax.numpy as jnp
from jax import lax
from jax.sharding import Mesh
from jax.sharding import PartitionSpec as P

CH_IN = 256
CH_OUT = 256
GROUPS = 8
ROWS = 8
WIDTH = 64


def linear_from(value, axis, step):
    count = lax.axis_size(axis)
    return lax.ppermute(value, axis, [(i + step, i) for i in range(count) if 0 <= i + step < count])


def haloed(block):
    deep = jnp.concatenate(
        [linear_from(block[:, -1:], "slab", -1), block, linear_from(block[:, :1], "slab", 1)], axis=1
    )
    return jnp.concatenate(
        [linear_from(deep[:, :, -1:], "rb", -1), deep, linear_from(deep[:, :, :1], "rb", 1)], axis=2
    )


def correlate(image, kernel, lhs_spec):
    return lax.conv_general_dilated(
        image,
        kernel,
        (1, 1, 1),
        ((0, 0), (0, 0), (1, 1)),
        dimension_numbers=(lhs_spec, "OIDHW", "NCDHW"),
        preferred_element_type=jnp.float32,
    )


def partner(value, axis, bit):
    count = lax.axis_size(axis)
    return lax.ppermute(value, axis, [(i, i ^ (1 << bit)) for i in range(count)])


def bit_of(axis, bit):
    return (lax.axis_index(axis) >> bit) % 2 == 1


def xor_gather(value, axis, bits):
    for bit in bits:
        other = partner(value, axis, bit)
        upper = bit_of(axis, bit)
        value = jnp.stack([jnp.where(upper, other, value), jnp.where(upper, value, other)])
    order = sorted(range(len(bits)), key=lambda j: -bits[len(bits) - 1 - j])
    value = jnp.transpose(value, order + list(range(len(bits), value.ndim)))
    return value.reshape((-1,) + value.shape[len(bits):])


def xor_scatter_sum(value, axis, bits):
    nbits = len(bits)
    value = value.reshape((2,) * nbits + value.shape[1:])
    for bit in bits:
        dim = nbits - 1 - bit
        upper = bit_of(axis, bit)
        low = lax.index_in_dim(value, 0, axis=dim, keepdims=True)
        high = lax.index_in_dim(value, 1, axis=dim, keepdims=True)
        keep = jnp.where(upper, high, low)
        sent = jnp.where(upper, low, high)
        value = keep + partner(sent, axis, bit)
    return value.reshape(value.shape[nbits:])


def xor_all_sum(value, axis, bits):
    for bit in bits:
        value = value + partner(value, axis, bit)
    return value


def per_device(activations, grad_out, weights):
    chan_local = activations.shape[0]
    depth_dev = activations.shape[1]
    rows_dev = weights.shape[1]
    n_rb = lax.axis_size("rb")
    n_slab = lax.axis_size("slab")
    depth_all = depth_dev * n_slab
    height_all = ROWS * n_rb

    all_in = xor_gather(activations, "grp", (1, 0, 2)).reshape(CH_IN, depth_dev, ROWS * WIDTH)
    both = jnp.concatenate([all_in, grad_out], axis=0).reshape(CH_IN + chan_local, depth_dev, ROWS, WIDTH)
    ext = haloed(both)
    whole_in = ext[:CH_IN]
    own_grad = ext[CH_IN:]

    group_weights = xor_gather(weights, "rb", (0, 2, 1))
    group_weights = jnp.transpose(group_weights, (1, 0, 2, 3)).reshape(27, n_rb * rows_dev, CH_IN)

    out_kernel = jnp.transpose(group_weights, (1, 2, 0)).reshape(chan_local, CH_IN, 3, 3, 3)
    output_sum = correlate(whole_in[None], out_kernel, "NCDHW")
    grad_padded = jnp.pad(grad_out.reshape(chan_local, depth_dev, ROWS, WIDTH), ((0, 0), (2, 2), (2, 2), (2, 2)))
    shifted_grad = jnp.stack([
        grad_padded[:, 2 - a:4 - a + depth_dev, 2 - b:4 - b + ROWS, 3 - c:3 - c + WIDTH]
        for a in range(3) for b in range(3) for c in range(3)
    ])
    filter_part = jnp.einsum(
        "tcdrw,idrw->tci", shifted_grad, whole_in, preferred_element_type=jnp.float32
    )
    in_kernel = jnp.transpose(group_weights[::-1], (2, 1, 0)).reshape(CH_IN, chan_local, 3, 3, 3)
    input_terms = correlate(own_grad[None], in_kernel, "NCDHW").reshape(GROUPS, chan_local, depth_dev, ROWS * WIDTH)
    input_sum = xor_scatter_sum(input_terms, "grp", (2, 0, 1))

    rows_terms = jnp.moveaxis(filter_part.reshape(27, n_rb, rows_dev, CH_IN), 1, 0)
    rows_part = xor_scatter_sum(rows_terms, "rb", (1, 0, 2))
    scale_factor = 1.0 / math.sqrt(depth_all * height_all * WIDTH)
    filter_grad = xor_all_sum(rows_part, "slab", (0, 1, 2)) * scale_factor
    out_map = output_sum.astype(jnp.bfloat16).reshape(chan_local, depth_dev, ROWS * WIDTH)
    grad_in = input_sum.astype(jnp.bfloat16)
    return (out_map, grad_in, filter_grad)


def solution(mesh):
    n_filt, n_slab = mesh.devices.shape
    grid = Mesh(mesh.devices.reshape(n_filt // GROUPS, GROUPS, n_slab), ("rb", "grp", "slab"))
    act_spec = P(("rb", "grp"), "slab", None)
    w_spec = P(None, ("rb", "grp"), None)
    in_specs = (act_spec, act_spec, w_spec)
    out_specs = (act_spec, act_spec, w_spec)
    return jax.shard_map(
        per_device, mesh=grid, in_specs=in_specs, out_specs=out_specs, check_vma=False
    )
```

```python
import math

import jax
import jax.numpy as jnp
from jax import lax
from jax.sharding import Mesh
from jax.sharding import PartitionSpec as P

CH_IN = 256
CH_OUT = 256
GROUPS = 8
ROWS = 8
WIDTH = 64


def linear_from(value, axis, step):
    count = lax.axis_size(axis)
    return lax.ppermute(value, axis, [(i + step, i) for i in range(count) if 0 <= i + step < count])


def haloed(block):
    deep = jnp.concatenate(
        [linear_from(block[:, -1:], "slab", -1), block, linear_from(block[:, :1], "slab", 1)], axis=1
    )
    return jnp.concatenate(
        [linear_from(deep[:, :, -1:], "rb", -1), deep, linear_from(deep[:, :, :1], "rb", 1)], axis=2
    )


def correlate(image, kernel, lhs_spec):
    return lax.conv_general_dilated(
        image,
        kernel,
        (1, 1, 1),
        ((0, 0), (0, 0), (1, 1)),
        dimension_numbers=(lhs_spec, "OIDHW", "NCDHW"),
        preferred_element_type=jnp.float32,
    )


def partner(value, axis, bit):
    count = lax.axis_size(axis)
    return lax.ppermute(value, axis, [(i, i ^ (1 << bit)) for i in range(count)])


def bit_of(axis, bit):
    return (lax.axis_index(axis) >> bit) % 2 == 1


def xor_gather(value, axis, bits):
    for bit in bits:
        other = partner(value, axis, bit)
        upper = bit_of(axis, bit)
        value = jnp.stack([jnp.where(upper, other, value), jnp.where(upper, value, other)])
    order = sorted(range(len(bits)), key=lambda j: -bits[len(bits) - 1 - j])
    value = jnp.transpose(value, order + list(range(len(bits), value.ndim)))
    return value.reshape((-1,) + value.shape[len(bits):])


def xor_scatter_sum(value, axis, bits):
    nbits = len(bits)
    value = value.reshape((2,) * nbits + value.shape[1:])
    for bit in bits:
        dim = nbits - 1 - bit
        upper = bit_of(axis, bit)
        low = lax.index_in_dim(value, 0, axis=dim, keepdims=True)
        high = lax.index_in_dim(value, 1, axis=dim, keepdims=True)
        keep = jnp.where(upper, high, low)
        sent = jnp.where(upper, low, high)
        value = keep + partner(sent, axis, bit)
    return value.reshape(value.shape[nbits:])


def xor_all_sum(value, axis, bits):
    for bit in bits:
        value = value + partner(value, axis, bit)
    return value


def merged_exchange(block, group_weights):
    bits = (1, 0, 2)
    nbits = len(bits)
    lanes = block.shape[-1]
    cols = group_weights.shape[2] // (1 << nbits)
    parts = group_weights.reshape(group_weights.shape[:2] + (2,) * nbits + (cols,))
    parts = jnp.moveaxis(parts, (2, 3, 4), (0, 1, 2))
    axes = [("dest", nbits - 1 - k) for k in range(nbits)]
    gathered_block = block
    for bit in bits:
        upper = bit_of("grp", bit)
        pos = axes.index(("dest", bit))
        low = lax.index_in_dim(parts, 0, axis=pos, keepdims=False)
        high = lax.index_in_dim(parts, 1, axis=pos, keepdims=False)
        keep = jnp.where(upper, high, low)
        sent = jnp.where(upper, low, high)
        axes.remove(("dest", bit))
        size = gathered_block.size
        payload = jnp.concatenate([gathered_block.reshape(-1, lanes), sent.reshape(-1, lanes)])
        received = partner(payload, "grp", bit)
        got_block = received[: size // lanes].reshape(gathered_block.shape)
        got_parts = received[size // lanes:].reshape(sent.shape)
        gathered_block = jnp.stack(
            [jnp.where(upper, got_block, gathered_block), jnp.where(upper, gathered_block, got_block)]
        )
        parts = jnp.stack([jnp.where(upper, got_parts, keep), jnp.where(upper, keep, got_parts)])
        axes = [("src", bit)] + axes
    order = sorted(range(nbits), key=lambda j: -bits[nbits - 1 - j])
    gathered_block = jnp.transpose(gathered_block, order + list(range(nbits, gathered_block.ndim)))
    gathered_block = gathered_block.reshape((-1,) + gathered_block.shape[nbits:])
    parts = jnp.transpose(parts, order + list(range(nbits, parts.ndim)))
    parts = parts.reshape((-1,) + parts.shape[nbits:])
    column_weights = jnp.moveaxis(parts, 0, 1)
    column_weights = column_weights.reshape((column_weights.shape[0], -1, cols))
    return gathered_block, column_weights


def per_device(activations, grad_out, weights):
    chan_local = activations.shape[0]
    depth_dev = activations.shape[1]
    rows_dev = weights.shape[1]
    n_rb = lax.axis_size("rb")
    n_slab = lax.axis_size("slab")
    depth_all = depth_dev * n_slab
    height_all = ROWS * n_rb

    group_weights = xor_gather(weights, "rb", (0, 2, 1))
    group_weights = jnp.transpose(group_weights, (1, 0, 2, 3)).reshape(27, n_rb * rows_dev, CH_IN)

    both = jnp.concatenate([activations, grad_out], axis=0)
    whole, column_weights = merged_exchange(both, group_weights)
    whole = whole.reshape(GROUPS, 2, chan_local, depth_dev, ROWS * WIDTH)
    whole = jnp.concatenate([whole[:, 0].reshape(CH_IN, depth_dev, ROWS, WIDTH),
                             whole[:, 1].reshape(CH_OUT, depth_dev, ROWS, WIDTH)])
    ext = haloed(whole)
    whole_in = ext[:CH_IN]
    whole_grad = ext[CH_IN:]

    out_kernel = jnp.transpose(group_weights, (1, 2, 0)).reshape(chan_local, CH_IN, 3, 3, 3)
    output_sum = correlate(whole_in[None], out_kernel, "NCDHW")
    grad_padded = jnp.pad(grad_out.reshape(chan_local, depth_dev, ROWS, WIDTH), ((0, 0), (2, 2), (2, 2), (2, 2)))
    shifted_grad = jnp.stack([
        grad_padded[:, 2 - a:4 - a + depth_dev, 2 - b:4 - b + ROWS, 3 - c:3 - c + WIDTH]
        for a in range(3) for b in range(3) for c in range(3)
    ])
    filter_part = jnp.einsum(
        "tcdrw,idrw->tci", shifted_grad, whole_in, preferred_element_type=jnp.float32
    )
    in_kernel = jnp.transpose(column_weights[::-1], (2, 1, 0)).reshape(chan_local, CH_OUT, 3, 3, 3)
    input_sum = correlate(whole_grad[None], in_kernel, "NCDHW")

    rows_terms = jnp.moveaxis(filter_part.reshape(27, n_rb, rows_dev, CH_IN), 1, 0)
    rows_part = xor_scatter_sum(rows_terms, "rb", (1, 0, 2))
    scale_factor = 1.0 / math.sqrt(depth_all * height_all * WIDTH)
    filter_grad = xor_all_sum(rows_part, "slab", (0, 1, 2)) * scale_factor
    out_map = output_sum.astype(jnp.bfloat16).reshape(chan_local, depth_dev, ROWS * WIDTH)
    grad_in = input_sum.astype(jnp.bfloat16).reshape(chan_local, depth_dev, ROWS * WIDTH)
    return (out_map, grad_in, filter_grad)


def solution(mesh):
    n_filt, n_slab = mesh.devices.shape
    grid = Mesh(mesh.devices.reshape(n_filt // GROUPS, GROUPS, n_slab), ("rb", "grp", "slab"))
    act_spec = P(("rb", "grp"), "slab", None)
    w_spec = P(None, ("rb", "grp"), None)
    in_specs = (act_spec, act_spec, w_spec)
    out_specs = (act_spec, act_spec, w_spec)
    return jax.shard_map(
        per_device, mesh=grid, in_specs=in_specs, out_specs=out_specs, check_vma=False
    )
```

```python
import math

import jax
import jax.numpy as jnp
from jax import lax
from jax.sharding import Mesh
from jax.sharding import PartitionSpec as P

CH_IN = 256
CH_OUT = 256
GROUPS = 8
ROWS = 8
WIDTH = 64


def linear_from(value, axis, step):
    count = lax.axis_size(axis)
    return lax.ppermute(value, axis, [(i + step, i) for i in range(count) if 0 <= i + step < count])


def haloed(block):
    deep = jnp.concatenate(
        [linear_from(block[:, -1:], "slab", -1), block, linear_from(block[:, :1], "slab", 1)], axis=1
    )
    return jnp.concatenate(
        [linear_from(deep[:, :, -1:], "rb", -1), deep, linear_from(deep[:, :, :1], "rb", 1)], axis=2
    )


def correlate(image, kernel, lhs_spec):
    return lax.conv_general_dilated(
        image,
        kernel,
        (1, 1, 1),
        ((0, 0), (0, 0), (1, 1)),
        dimension_numbers=(lhs_spec, "OIDHW", "NCDHW"),
        preferred_element_type=jnp.float32,
    )


def partner(value, axis, bit):
    count = lax.axis_size(axis)
    return lax.ppermute(value, axis, [(i, i ^ (1 << bit)) for i in range(count)])


def bit_of(axis, bit):
    return (lax.axis_index(axis) >> bit) % 2 == 1


def xor_gather(value, axis, bits):
    for bit in bits:
        value = jnp.stack([value, partner(value, axis, bit)])
    order = sorted(range(len(bits)), key=lambda j: -bits[len(bits) - 1 - j])
    value = jnp.transpose(value, order + list(range(len(bits), value.ndim)))
    value = value.reshape((-1,) + value.shape[len(bits):])
    return jnp.take(value, jnp.arange(value.shape[0]) ^ lax.axis_index(axis), axis=0)


def xor_scatter_sum(value, axis, bits):
    nbits = len(bits)
    value = value.reshape((2,) * nbits + value.shape[1:])
    for bit in bits:
        dim = nbits - 1 - bit
        upper = bit_of(axis, bit)
        low = lax.index_in_dim(value, 0, axis=dim, keepdims=True)
        high = lax.index_in_dim(value, 1, axis=dim, keepdims=True)
        keep = jnp.where(upper, high, low)
        sent = jnp.where(upper, low, high)
        value = keep + partner(sent, axis, bit)
    return value.reshape(value.shape[nbits:])


def xor_all_sum(value, axis, bits):
    for bit in bits:
        value = value + partner(value, axis, bit)
    return value


def per_device(activations, grad_out, weights):
    chan_local = activations.shape[0]
    depth_dev = activations.shape[1]
    rows_dev = weights.shape[1]
    n_rb = lax.axis_size("rb")
    n_slab = lax.axis_size("slab")
    depth_all = depth_dev * n_slab
    height_all = ROWS * n_rb

    all_in = xor_gather(activations, "grp", (1, 0, 2)).reshape(CH_IN, depth_dev, ROWS * WIDTH)
    both = jnp.concatenate([all_in, grad_out], axis=0).reshape(CH_IN + chan_local, depth_dev, ROWS, WIDTH)
    ext = haloed(both)
    whole_in = ext[:CH_IN]
    own_grad = ext[CH_IN:]

    group_weights = xor_gather(weights, "rb", (0, 2, 1))
    group_weights = jnp.transpose(group_weights, (1, 0, 2, 3)).reshape(27, n_rb * rows_dev, CH_IN)

    out_kernel = jnp.transpose(group_weights, (1, 2, 0)).reshape(chan_local, CH_IN, 3, 3, 3)
    output_sum = correlate(whole_in[None], out_kernel, "NCDHW")
    grad_kernel = grad_out.reshape(chan_local, 1, depth_dev, ROWS, WIDTH)
    filter_terms = correlate(whole_in[:, None], grad_kernel, "NCDHW")
    filter_part = jnp.transpose(filter_terms.reshape(CH_IN, chan_local, 27), (2, 1, 0))
    in_kernel = jnp.transpose(group_weights[::-1], (2, 1, 0)).reshape(CH_IN, chan_local, 3, 3, 3)
    input_terms = correlate(own_grad[None], in_kernel, "NCDHW").reshape(GROUPS, chan_local, depth_dev, ROWS * WIDTH)
    input_sum = xor_scatter_sum(input_terms, "grp", (2, 0, 1))

    rows_terms = jnp.moveaxis(filter_part.reshape(27, n_rb, rows_dev, CH_IN), 1, 0)
    rows_part = xor_scatter_sum(rows_terms, "rb", (1, 0, 2))
    scale_factor = 1.0 / math.sqrt(depth_all * height_all * WIDTH)
    filter_grad = xor_all_sum(rows_part, "slab", (0, 1, 2)) * scale_factor
    out_map = output_sum.astype(jnp.bfloat16).reshape(chan_local, depth_dev, ROWS * WIDTH)
    grad_in = input_sum.astype(jnp.bfloat16)
    return (out_map, grad_in, filter_grad)


def solution(mesh):
    n_filt, n_slab = mesh.devices.shape
    grid = Mesh(mesh.devices.reshape(n_filt // GROUPS, GROUPS, n_slab), ("rb", "grp", "slab"))
    act_spec = P(("rb", "grp"), "slab", None)
    w_spec = P(None, ("rb", "grp"), None)
    in_specs = (act_spec, act_spec, w_spec)
    out_specs = (act_spec, act_spec, w_spec)
    return jax.shard_map(
        per_device, mesh=grid, in_specs=in_specs, out_specs=out_specs, check_vma=False
    )
```

```python
import math

import jax
import jax.numpy as jnp
from jax import lax
from jax.sharding import Mesh
from jax.sharding import PartitionSpec as P

CH_IN = 256
CH_OUT = 256
GROUPS = 8
ROWS = 8
WIDTH = 64


def linear_from(value, axis, step):
    count = lax.axis_size(axis)
    return lax.ppermute(value, axis, [(i + step, i) for i in range(count) if 0 <= i + step < count])


def haloed(block):
    deep = jnp.concatenate(
        [linear_from(block[:, -1:], "slab", -1), block, linear_from(block[:, :1], "slab", 1)], axis=1
    )
    return jnp.concatenate(
        [linear_from(deep[:, :, -1:], "rb", -1), deep, linear_from(deep[:, :, :1], "rb", 1)], axis=2
    )


def correlate(image, kernel, lhs_spec):
    return lax.conv_general_dilated(
        image,
        kernel,
        (1, 1, 1),
        ((0, 0), (0, 0), (1, 1)),
        dimension_numbers=(lhs_spec, "OIDHW", "NCDHW"),
        preferred_element_type=jnp.float32,
    )


def partner(value, axis, bit):
    count = lax.axis_size(axis)
    return lax.ppermute(value, axis, [(i, i ^ (1 << bit)) for i in range(count)])


def bit_of(axis, bit):
    return (lax.axis_index(axis) >> bit) % 2 == 1


def xor_gather(value, axis, bits):
    for bit in bits:
        other = partner(value, axis, bit)
        upper = bit_of(axis, bit)
        value = jnp.stack([jnp.where(upper, other, value), jnp.where(upper, value, other)])
    order = sorted(range(len(bits)), key=lambda j: -bits[len(bits) - 1 - j])
    value = jnp.transpose(value, order + list(range(len(bits), value.ndim)))
    return value.reshape((-1,) + value.shape[len(bits):])


def xor_scatter_sum(value, axis, bits):
    nbits = len(bits)
    value = value.reshape((2,) * nbits + value.shape[1:])
    for bit in bits:
        dim = nbits - 1 - bit
        mine = (lax.axis_index(axis) >> bit) % 2
        keep = lax.dynamic_index_in_dim(value, mine, axis=dim, keepdims=True)
        sent = lax.dynamic_index_in_dim(value, 1 - mine, axis=dim, keepdims=True)
        value = keep + partner(sent, axis, bit)
    return value.reshape(value.shape[nbits:])


def xor_all_sum(value, axis, bits):
    for bit in bits:
        value = value + partner(value, axis, bit)
    return value


def per_device(activations, grad_out, weights):
    chan_local = activations.shape[0]
    depth_dev = activations.shape[1]
    rows_dev = weights.shape[1]
    n_rb = lax.axis_size("rb")
    n_slab = lax.axis_size("slab")
    depth_all = depth_dev * n_slab
    height_all = ROWS * n_rb

    all_in = xor_gather(activations, "grp", (1, 0, 2)).reshape(CH_IN, depth_dev, ROWS * WIDTH)
    both = jnp.concatenate([all_in, grad_out], axis=0).reshape(CH_IN + chan_local, depth_dev, ROWS, WIDTH)
    ext = haloed(both)
    whole_in = ext[:CH_IN]
    own_grad = ext[CH_IN:]

    group_weights = xor_gather(weights, "rb", (0, 2, 1))
    group_weights = jnp.transpose(group_weights, (1, 0, 2, 3)).reshape(27, n_rb * rows_dev, CH_IN)

    out_kernel = jnp.transpose(group_weights, (1, 2, 0)).reshape(chan_local, CH_IN, 3, 3, 3)
    output_sum = correlate(whole_in[None], out_kernel, "NCDHW")
    grad_kernel = grad_out.reshape(chan_local, 1, depth_dev, ROWS, WIDTH)
    filter_terms = correlate(whole_in[:, None], grad_kernel, "NCDHW")
    filter_part = jnp.transpose(filter_terms.reshape(CH_IN, chan_local, 27), (2, 1, 0))
    in_kernel = jnp.transpose(group_weights[::-1], (2, 1, 0)).reshape(CH_IN, chan_local, 3, 3, 3)
    input_terms = correlate(own_grad[None], in_kernel, "NCDHW").reshape(GROUPS, chan_local, depth_dev, ROWS * WIDTH)
    input_sum = xor_scatter_sum(input_terms, "grp", (2, 0, 1))

    rows_terms = jnp.moveaxis(filter_part.reshape(27, n_rb, rows_dev, CH_IN), 1, 0)
    rows_part = xor_scatter_sum(rows_terms, "rb", (1, 0, 2))
    scale_factor = 1.0 / math.sqrt(depth_all * height_all * WIDTH)
    filter_grad = xor_all_sum(rows_part, "slab", (0, 1, 2)) * scale_factor
    out_map = output_sum.astype(jnp.bfloat16).reshape(chan_local, depth_dev, ROWS * WIDTH)
    grad_in = input_sum.astype(jnp.bfloat16)
    return (out_map, grad_in, filter_grad)


def solution(mesh):
    n_filt, n_slab = mesh.devices.shape
    grid = Mesh(mesh.devices.reshape(n_filt // GROUPS, GROUPS, n_slab), ("rb", "grp", "slab"))
    act_spec = P(("rb", "grp"), "slab", None)
    w_spec = P(None, ("rb", "grp"), None)
    in_specs = (act_spec, act_spec, w_spec)
    out_specs = (act_spec, act_spec, w_spec)
    return jax.shard_map(
        per_device, mesh=grid, in_specs=in_specs, out_specs=out_specs, check_vma=False
    )
```
